512 devices in a mesh: blk: 64 (over y, z_lo, core), head: 8 (over z_hi, x).
Axes of the slice: x: 4, y: 8, z: 8 (z_hi: 2, z_lo: 4; z = z_hi * 4 + z_lo), core: 2. Of those that a mesh axis runs over, the one named last changes fastest.
Arguments:
- query_rows: bfloat16 [16384, 5120], P(('blk', 'head')), may hold values from -12 to 12
- key_rows: bfloat16 [16384, 1024], P(('blk', 'head')), may hold values from -6 to 6
- value_rows: bfloat16 [16384, 1024], P(('blk', 'head')), may hold values from -6 to 6
- out_grads: bfloat16 [16384, 5120], P(('blk', 'head')), may hold values from -1.75 to 1.75
- lengths: int32 [128], replicated, may hold values from 1 to 128, as said below
- ancestors: int32 [128, 5], replicated, may hold values from -1 to 126, as said below
Outputs:
- query_grads: bfloat16 [16384, 5120], P(('blk', 'head'))
- key_grads: bfloat16 [16384, 1024], P(('blk', 'head'))
- value_grads: bfloat16 [16384, 1024], P(('blk', 'head'))
The draws below stay inside these ranges and needn't reach their ends.
Inputs may be any that keep to these rules, and one draw needn't show every extreme that they name: `ancestors`: row t lists, in increasing order and followed by -1 entries, the tiles above tile t in the trie other than the 1 prompt tiles, which form a chain above every other tile. Every listed tile is a non-prompt tile below t that lies on the device of tile t or on one of the 2 devices before it; the last listed tile is the parent of t, and the row of a listed tile is a prefix of row t. Rows of prompt tiles are all -1. Some row has no -1 entry. On the devices before the last 3, the last tile of each device not a multiple of 3 has as parent the last tile of the device before, and the second-to-last tile of each device d >= 2 with d % 3 != 1 has as parent the second-to-last tile of the device before; those of the other devices have no non-prompt ancestor. lengths[t] slots of tile t hold tokens, the rest is padding; tile 0 is full.
All inputs are finite; a program needn't handle non-finite values.
Results may differ from the reference program's by a relative error of at most 0.0052.
Values may be sent and summed in bfloat16 or wider, within the bound.
No kernel may reach another device: no remote copies, remote signals or barrier semaphores. Data moves between devices by JAX's collectives and lax.ppermute only.
A program may use at most 64 MiB of HBM per device.

```python
import jax
import jax.numpy as jnp
from jax import lax

HD = 128
QH = 40
KVH = 8
TILE = 128
SPAN_DEV = 2
PROMPT_TILES = 1
TILES_DEV = 2
TILES = 128
TOKENS = 16384
ANC = 5
KEYT = 7


def draw_query_rows(key, part):
    array_shape = (TOKENS, QH * HD)
    drawn = jnp.clip(jax.random.normal(jax.random.fold_in(key, 1), array_shape, jnp.float32), -6.0, 6.0)
    return drawn.astype(jnp.bfloat16)


def draw_key_rows(key, part):
    array_shape = (TOKENS, KVH * HD)
    drawn = jnp.clip(jax.random.normal(jax.random.fold_in(key, 2), array_shape, jnp.float32), -6.0, 6.0)
    return drawn.astype(jnp.bfloat16)


def draw_lengths(key, part):
    whole = jax.random.randint(jax.random.fold_in(key, 3), (TILES,), 0, 2, dtype=jnp.int32)
    partial_len = jax.random.randint(jax.random.fold_in(key, 4), (TILES,), 1, TILE + 1, dtype=jnp.int32)
    result = jnp.where(whole == 1, TILE, partial_len).astype(jnp.int32)
    return result.at[0].set(TILE).astype(jnp.int32)


def draw_ancestors(key, part):
    forced_first = (TILES // TILES_DEV - 1 - SPAN_DEV) * TILES_DEV
    slot_index = jnp.arange(ANC, dtype=jnp.int32)

    def step_tile(tile_id, state):
        table, counts, oldest = state
        tile_id = jnp.asarray(tile_id).astype(jnp.int32)
        seeded = jax.random.fold_in(key, tile_id)
        branch_kind = jax.random.randint(jax.random.fold_in(seeded, 1), (), 0, 4, dtype=jnp.int32)
        backward = jax.random.randint(jax.random.fold_in(seeded, 2), (), 1, ANC + 1, dtype=jnp.int32)
        window_start = jnp.maximum((tile_id // TILES_DEV - SPAN_DEV) * TILES_DEV, PROMPT_TILES).astype(jnp.int32)
        in_chain = (tile_id > forced_first) & (tile_id <= forced_first + ANC)
        device_of = tile_id // TILES_DEV
        within = tile_id % TILES_DEV
        phase = device_of % 3
        periodic = tile_id < forced_first
        last_slot = within == TILES_DEV - 1
        second_slot = within == TILES_DEV - 2
        force_link = periodic & (last_slot & (phase != 0) | second_slot & (phase != 1) & (device_of >= 1))
        force_root = periodic & (last_slot & (phase == 0) | second_slot & (phase == 1))
        parent = jnp.where(branch_kind == 3, tile_id - backward, tile_id - 1)
        parent = jnp.where(in_chain, tile_id - 1, parent)
        parent = jnp.where(force_link, tile_id - TILES_DEV, parent)
        parent = jnp.maximum(parent, 0).astype(jnp.int32)
        usable = (branch_kind > 0) & (parent >= window_start) & (oldest[parent] >= window_start) & (counts[parent] < ANC)
        usable = jnp.where(tile_id == forced_first, False, jnp.where(in_chain, True, usable))
        usable = jnp.where(force_root, False, jnp.where(force_link, True, usable))
        place = counts[parent]
        row = jnp.where(usable, table[parent], -jnp.ones((ANC,), jnp.int32))
        row = jnp.where(usable & (slot_index == place), parent, row).astype(jnp.int32)
        table = table.at[tile_id].set(row)
        counts = counts.at[tile_id].set(jnp.where(usable, place + 1, 0).astype(jnp.int32))
        oldest = oldest.at[tile_id].set(jnp.where(usable, oldest[parent], tile_id).astype(jnp.int32))
        return (table, counts, oldest)
    start_state = (-jnp.ones((TILES, ANC), jnp.int32), jnp.zeros((TILES,), jnp.int32), jnp.arange(TILES, dtype=jnp.int32))
    table, counts, oldest = lax.fori_loop(PROMPT_TILES, TILES, step_tile, start_state)
    return table.astype(jnp.int32)


def shard_levels(key, dims, shards, smallest, high):
    gain = 1.0
    for dim, blocks in shards:
        heights = jax.random.uniform(jax.random.fold_in(jax.random.fold_in(key, 6), dim), (blocks,), jnp.float32, smallest / len(shards), high / len(shards))
        gain = gain * jnp.repeat(jnp.exp(heights), dims[dim] // blocks).reshape((-1,) + (1,) * (len(dims) - 1 - dim))
    return gain


def bell_draw(own_key, extent, spread, most, cuts=(), kind=jnp.bfloat16):
    values = spread * jax.random.normal(own_key, extent, jnp.float32)
    if cuts:
        values = values * shard_levels(own_key, extent, cuts, -0.22, 0.18)
    return jnp.clip(values, -most, most).astype(kind)


def setup_inputs(seed: int = 0) -> dict:
    streams_of = jax.random.split(jax.random.key(seed), 7)
    query_rows = draw_query_rows(jax.random.fold_in(streams_of[6], 71), 0)
    key_rows = draw_key_rows(jax.random.fold_in(streams_of[6], 71), 0)
    value_rows = bell_draw(streams_of[2], (TOKENS, KVH * HD), 1.0, 6.0, ((0, 512),))
    out_grads = bell_draw(streams_of[3], (TOKENS, QH * HD), 0.3, 1.75, ((0, 512),))
    lengths = draw_lengths(jax.random.fold_in(streams_of[6], 71), 0)
    ancestors = draw_ancestors(jax.random.fold_in(streams_of[6], 71), 0)
    return dict(query_rows=query_rows, key_rows=key_rows, value_rows=value_rows, out_grads=out_grads, lengths=lengths, ancestors=ancestors)


def visible_mask(tile_id, tile_ids, listed, lengths):
    position = jnp.arange(TILE, dtype=jnp.int32)
    slot_ok = jnp.concatenate([jnp.arange(PROMPT_TILES, dtype=jnp.int32) < tile_id, listed >= 0, jnp.ones((1,), bool)])
    key_len = jnp.take(lengths, jnp.maximum(tile_ids, 0).astype(jnp.int32))
    key_ok = slot_ok[:, None] & (position[None, :] < key_len[:, None])
    own_slot = jnp.arange(KEYT) == KEYT - 1
    causal = position[None, None, :] <= position[:, None, None]
    allowed = key_ok[None, :, :] & (causal | ~own_slot[None, :, None])
    return allowed.reshape(TILE, KEYT * TILE)


def reference(query_rows, key_rows, value_rows, out_grads, lengths, ancestors):
    group_size = QH // KVH
    scaling = HD ** -0.5
    query_tiles = query_rows.reshape(TILES, TILE, KVH, group_size, HD)
    grad_tiles = out_grads.reshape(TILES, TILE, KVH, group_size, HD)
    key_tiles = key_rows.reshape(TILES, TILE, KVH, HD)
    value_tiles = value_rows.reshape(TILES, TILE, KVH, HD)
    prompt_ids = jnp.arange(PROMPT_TILES, dtype=jnp.int32)

    def one_tile(carry, tile_id):
        key_sum, value_sum = carry
        listed = ancestors[tile_id]
        tile_ids = jnp.concatenate([prompt_ids, listed, tile_id[None]]).astype(jnp.int32)
        safe_ids = jnp.maximum(tile_ids, 0).astype(jnp.int32)
        allowed = visible_mask(tile_id, tile_ids, listed, lengths)
        live_rows = jnp.arange(TILE, dtype=jnp.int32) < lengths[tile_id]
        key_block = key_tiles[safe_ids].reshape(KEYT * TILE, KVH, HD).astype(jnp.float32)
        value_block = value_tiles[safe_ids].reshape(KEYT * TILE, KVH, HD).astype(jnp.float32)
        queries = query_tiles[tile_id].astype(jnp.float32)
        grads_out = grad_tiles[tile_id].astype(jnp.float32)
        scores = jnp.einsum("igrd,jgd->grij", queries, key_block) * scaling
        scores = jnp.where(allowed, scores, -jnp.inf)
        row_max = jnp.max(scores, axis=-1, keepdims=True)
        log_total = row_max + jnp.log(jnp.sum(jnp.exp(scores - row_max), axis=-1, keepdims=True))
        weights = jnp.where(allowed & live_rows[:, None], jnp.exp(scores - log_total), 0.0)
        weight_grads = jnp.einsum("igrd,jgd->grij", grads_out, value_block)
        row_dot = jnp.sum(weights * weight_grads, axis=-1, keepdims=True)
        score_grads = (weights * (weight_grads - row_dot)).astype(jnp.bfloat16)
        score_grads = lax.optimization_barrier(score_grads).astype(jnp.float32)
        weights_low = weights.astype(jnp.bfloat16)
        weights_low = lax.optimization_barrier(weights_low).astype(jnp.float32)
        tile_query_grads = (jnp.einsum("grij,jgd->igrd", score_grads, key_block) * scaling).astype(jnp.bfloat16)
        key_part = jnp.einsum("grij,igrd->jgd", score_grads, queries)
        value_part = jnp.einsum("grij,igrd->jgd", weights_low, grads_out)
        key_sum = key_sum.at[safe_ids].add(key_part.reshape(KEYT, TILE, KVH * HD))
        value_sum = value_sum.at[safe_ids].add(value_part.reshape(KEYT, TILE, KVH * HD))
        return (key_sum, value_sum), tile_query_grads.reshape(TILE, QH * HD)

    empty = jnp.zeros((TILES, TILE, KVH * HD), jnp.float32)
    (key_sum, value_sum), query_parts = lax.scan(one_tile, (empty, empty), jnp.arange(TILES, dtype=jnp.int32))
    query_grads = query_parts.reshape(TOKENS, QH * HD)
    key_grads = (key_sum * scaling).astype(jnp.bfloat16).reshape(TOKENS, KVH * HD)
    value_grads = value_sum.astype(jnp.bfloat16).reshape(TOKENS, KVH * HD)
    return (query_grads, key_grads, value_grads)
```

```python
import jax
import jax.numpy as jnp
from jax import lax
from jax.sharding import PartitionSpec as P

HD = 128
TILE = 128
SPAN_DEV = 2
PROMPT_TILES = 1
ANC = 5
KEYT = 7


def spread(value, axis, source):
    kept = jnp.where(lax.axis_index(axis) == source, value, 0).astype(value.dtype)
    return lax.psum(kept, axis)


def tree_levels(size):
    levels = []
    stride = 1
    for radix in (2, 4):
        if size % (stride * radix) == 0:
            levels.append((stride, radix))
            stride *= radix
    if size // stride > 1:
        levels.append((stride, size // stride))
    return levels


def tree_spread(value, axis):
    size = lax.axis_size(axis)
    index = lax.axis_index(axis)
    for stride, radix in tree_levels(size):
        got = [
            lax.ppermute(value, axis, [(j, j + k * stride) for j in range(stride)])
            for k in range(1, radix)
        ]
        arrived = got[0]
        for extra in got[1:]:
            arrived = arrived + extra
        value = jnp.where(index < stride, value, arrived)
    return value


def tree_total(value, axis):
    size = lax.axis_size(axis)
    for stride, radix in reversed(tree_levels(size)):
        got = [
            lax.ppermute(value, axis, [(j + k * stride, j) for j in range(stride)])
            for k in range(1, radix)
        ]
        for extra in got:
            value = value + extra
    return value


def passed_along(block, axis, distance):
    devices = range(lax.axis_size(axis))
    route = [(i - distance, i) for i in devices if i - distance in devices]
    return lax.ppermute(block, axis, route)


def visible_mask(tile_id, tile_ids, listed, lengths):
    position = jnp.arange(TILE, dtype=jnp.int32)
    slot_ok = jnp.concatenate(
        [jnp.arange(PROMPT_TILES, dtype=jnp.int32) < tile_id, listed >= 0, jnp.ones((1,), bool)]
    )
    key_len = jnp.take(lengths, jnp.maximum(tile_ids, 0))
    key_ok = slot_ok[:, None] & (position[None, :] < key_len[:, None])
    own_slot = jnp.arange(KEYT) == KEYT - 1
    causal = position[None, None, :] <= position[:, None, None]
    allowed = key_ok[None, :, :] & (causal | ~own_slot[None, :, None])
    return allowed.reshape(TILE, KEYT * TILE)


def tile_backward(queries, grads_out, key_block, value_block, allowed, live_rows, scaling):
    scores = (
        jnp.einsum("igrd,jgd->grij", queries, key_block, preferred_element_type=jnp.float32)
        * scaling
    )
    scores = jnp.where(allowed, scores, -jnp.inf)
    row_max = jnp.max(scores, axis=-1, keepdims=True)
    log_total = row_max + jnp.log(jnp.sum(jnp.exp(scores - row_max), axis=-1, keepdims=True))
    weights = jnp.where(allowed & live_rows[:, None], jnp.exp(scores - log_total), 0.0)
    weight_grads = jnp.einsum(
        "igrd,jgd->grij", grads_out, value_block, preferred_element_type=jnp.float32
    )
    row_dot = jnp.sum(weights * weight_grads, axis=-1, keepdims=True)
    score_grads = (weights * (weight_grads - row_dot)).astype(jnp.bfloat16)
    weights_low = weights.astype(jnp.bfloat16)
    query_part = (
        jnp.einsum("grij,jgd->igrd", score_grads, key_block, preferred_element_type=jnp.float32)
        * scaling
    )
    key_part = jnp.einsum(
        "grij,igrd->jgd", score_grads, queries, preferred_element_type=jnp.float32
    )
    value_part = jnp.einsum(
        "grij,igrd->jgd", weights_low, grads_out, preferred_element_type=jnp.float32
    )
    return (query_part.astype(jnp.bfloat16), key_part, value_part)


def shards(query_rows, key_rows, value_rows, out_grads, lengths, ancestors):
    head_query, head_key, head_value, head_grad = (
        lax.all_to_all(query_rows, "head", split_axis=1, concat_axis=0, tiled=True),
        lax.all_to_all(key_rows, "head", split_axis=1, concat_axis=0, tiled=True),
        lax.all_to_all(value_rows, "head", split_axis=1, concat_axis=0, tiled=True),
        lax.all_to_all(out_grads, "head", split_axis=1, concat_axis=0, tiled=True),
    )
    row_count = head_query.shape[0]
    tiles_here = row_count // TILE
    kv_width = head_key.shape[1]
    kv_heads = kv_width // HD
    group_size = head_query.shape[1] // kv_width
    scaling = HD ** (-0.5)
    block_index = lax.axis_index("blk")
    first_tile = block_index * tiles_here
    window_first = (block_index - SPAN_DEV) * tiles_here
    window_slots = (SPAN_DEV + 1) * tiles_here
    own_states = jnp.concatenate(
        [
            head_key.reshape(tiles_here, TILE, kv_width),
            head_value.reshape(tiles_here, TILE, kv_width),
        ],
        axis=2,
    )
    my_lists = lax.dynamic_slice_in_dim(ancestors, first_tile, tiles_here, 0)
    prompt_ids = jnp.arange(PROMPT_TILES, dtype=jnp.int32)
    pieces = [tree_spread(own_states[:PROMPT_TILES], "blk")]
    for offset in range(SPAN_DEV, 0, -1):
        pieces.append(passed_along(own_states, "blk", offset))
    pieces.append(own_states)
    table = jnp.concatenate(pieces, axis=0)
    slot_index = jnp.arange(window_slots, dtype=jnp.int32)
    prompt_sum = jnp.zeros((PROMPT_TILES, TILE, 2 * kv_width), jnp.float32)
    near_sum = jnp.zeros((window_slots, TILE * 2 * kv_width), jnp.float32)
    query_parts = []
    for local in range(tiles_here):
        tile_id = first_tile + local
        listed = my_lists[local]
        tile_ids = jnp.concatenate([prompt_ids, listed, tile_id[None]])
        near_rows = jnp.where(listed >= 0, PROMPT_TILES + listed - window_first, 0)
        own_row = jnp.full((1,), PROMPT_TILES + SPAN_DEV * tiles_here + local, jnp.int32)
        table_rows = jnp.concatenate([prompt_ids, near_rows, own_row])
        chosen = jnp.take(table, table_rows, axis=0)
        key_block = chosen[:, :, :kv_width].reshape(KEYT * TILE, kv_heads, HD)
        value_block = chosen[:, :, kv_width:].reshape(KEYT * TILE, kv_heads, HD)
        allowed = visible_mask(tile_id, tile_ids, listed, lengths)
        live_rows = jnp.arange(TILE, dtype=jnp.int32) < lengths[tile_id]
        tile_query = head_query[local * TILE : (local + 1) * TILE].reshape(
            TILE, kv_heads, group_size, HD
        )
        tile_grad = head_grad[local * TILE : (local + 1) * TILE].reshape(
            TILE, kv_heads, group_size, HD
        )
        query_part, key_part, value_part = tile_backward(
            tile_query, tile_grad, key_block, value_block, allowed, live_rows, scaling
        )
        query_parts.append(query_part.reshape(TILE, group_size * kv_width))
        tile_terms = jnp.concatenate(
            [key_part.reshape(KEYT, TILE, kv_width), value_part.reshape(KEYT, TILE, kv_width)],
            axis=2,
        )
        prompt_sum = prompt_sum + tile_terms[:PROMPT_TILES]
        window_ids = jnp.concatenate(
            [listed - window_first, jnp.full((1,), SPAN_DEV * tiles_here + local, jnp.int32)]
        )
        usable = jnp.concatenate([listed >= 0, jnp.ones((1,), bool)])
        placing = ((window_ids[:, None] == slot_index[None, :]) & usable[:, None]).astype(
            jnp.float32
        )
        near_sum = near_sum + jnp.einsum(
            "sw,sx->wx",
            placing,
            tile_terms[PROMPT_TILES:].reshape(ANC + 1, TILE * 2 * kv_width),
            precision=lax.Precision.HIGHEST,
        )
    root_total = tree_total(prompt_sum, "blk")
    near_parts = near_sum.reshape(SPAN_DEV + 1, tiles_here, TILE, 2 * kv_width)
    total = near_parts[SPAN_DEV]
    for offset in range(1, SPAN_DEV + 1):
        total = total + passed_along(near_parts[SPAN_DEV - offset], "blk", -offset)
    total = total.at[:PROMPT_TILES].add(jnp.where(block_index == 0, root_total, 0.0))
    key_out = (total[:, :, :kv_width] * scaling).astype(jnp.bfloat16).reshape(row_count, kv_width)
    value_out = total[:, :, kv_width:].astype(jnp.bfloat16).reshape(row_count, kv_width)
    query_out = jnp.concatenate(query_parts, axis=0)
    query_grads, key_grads, value_grads = (
        lax.all_to_all(query_out, "head", split_axis=0, concat_axis=1, tiled=True),
        lax.all_to_all(key_out, "head", split_axis=0, concat_axis=1, tiled=True),
        lax.all_to_all(value_out, "head", split_axis=0, concat_axis=1, tiled=True),
    )
    return (query_grads, key_grads, value_grads)


def solution(mesh):
    placed = (
        P(("blk", "head"), None),
        P(("blk", "head"), None),
        P(("blk", "head"), None),
        P(("blk", "head"), None),
        P(),
        P(),
    )
    return jax.shard_map(
        shards,
        mesh=mesh,
        in_specs=placed,
        out_specs=(P(("blk", "head"), None), P(("blk", "head"), None), P(("blk", "head"), None)),
        check_vma=False,
    )
```

```python
import jax
import jax.numpy as jnp
from jax import lax
from jax.sharding import PartitionSpec as P

HD = 128
TILE = 128
SPAN_DEV = 2
PROMPT_TILES = 1
ANC = 5
KEYT = 7


def spread(value, axis, source):
    kept = jnp.where(lax.axis_index(axis) == source, value, 0).astype(value.dtype)
    return lax.psum(kept, axis)


def tree_levels(size):
    levels = []
    stride = 1
    for radix in (2, 4):
        if size % (stride * radix) == 0:
            levels.append((stride, radix))
            stride *= radix
    if size // stride > 1:
        levels.append((stride, size // stride))
    return levels


def tree_spread(value, axis):
    size = lax.axis_size(axis)
    index = lax.axis_index(axis)
    for stride, radix in tree_levels(size):
        got = [
            lax.ppermute(value, axis, [(j, j + k * stride) for j in range(stride)])
            for k in range(1, radix)
        ]
        arrived = got[0]
        for extra in got[1:]:
            arrived = arrived + extra
        value = jnp.where(index < stride, value, arrived)
    return value


def binary_levels(size):
    levels = []
    for stride, radix in tree_levels(size):
        if radix & (radix - 1) == 0:
            while radix > 1:
                levels.append((stride, 2))
                stride *= 2
                radix //= 2
        else:
            levels.append((stride, radix))
    return levels


def tree_total(value, axis):
    size = lax.axis_size(axis)
    for stride, radix in reversed(tree_levels(size)[:-1] + binary_levels(size)[-3:]):
        got = [
            lax.ppermute(value, axis, [(j + k * stride, j) for j in range(stride)])
            for k in range(1, radix)
        ]
        for extra in got:
            value = value + extra
    return value


def passed_along(block, axis, distance):
    devices = range(lax.axis_size(axis))
    route = [(i - distance, i) for i in devices if i - distance in devices]
    return lax.ppermute(block, axis, route)


def visible_mask(tile_id, tile_ids, listed, lengths):
    position = jnp.arange(TILE, dtype=jnp.int32)
    slot_ok = jnp.concatenate(
        [jnp.arange(PROMPT_TILES, dtype=jnp.int32) < tile_id, listed >= 0, jnp.ones((1,), bool)]
    )
    key_len = jnp.take(lengths, jnp.maximum(tile_ids, 0))
    key_ok = slot_ok[:, None] & (position[None, :] < key_len[:, None])
    own_slot = jnp.arange(KEYT) == KEYT - 1
    causal = position[None, None, :] <= position[:, None, None]
    allowed = key_ok[None, :, :] & (causal | ~own_slot[None, :, None])
    return allowed.reshape(TILE, KEYT * TILE)


def tile_backward(queries, grads_out, key_block, value_block, allowed, live_rows, scaling):
    scores = (
        jnp.einsum("igrd,jgd->grij", queries, key_block, preferred_element_type=jnp.float32)
        * scaling
    )
    scores = jnp.where(allowed, scores, -jnp.inf)
    row_max = jnp.max(scores, axis=-1, keepdims=True)
    log_total = row_max + jnp.log(jnp.sum(jnp.exp(scores - row_max), axis=-1, keepdims=True))
    weights = jnp.where(allowed & live_rows[:, None], jnp.exp(scores - log_total), 0.0)
    weight_grads = jnp.einsum(
        "igrd,jgd->grij", grads_out, value_block, preferred_element_type=jnp.float32
    )
    row_dot = jnp.sum(weights * weight_grads, axis=-1, keepdims=True)
    score_grads = (weights * (weight_grads - row_dot)).astype(jnp.bfloat16)
    weights_low = weights.astype(jnp.bfloat16)
    query_part = (
        jnp.einsum("grij,jgd->igrd", score_grads, key_block, preferred_element_type=jnp.float32)
        * scaling
    )
    key_part = jnp.einsum(
        "grij,igrd->jgd", score_grads, queries, preferred_element_type=jnp.float32
    )
    value_part = jnp.einsum(
        "grij,igrd->jgd", weights_low, grads_out, preferred_element_type=jnp.float32
    )
    return (query_part.astype(jnp.bfloat16), key_part, value_part)


def shards(query_rows, key_rows, value_rows, out_grads, lengths, ancestors):
    head_groups = lax.axis_size("head")
    width_q = query_rows.shape[1] // head_groups
    width_k = key_rows.shape[1] // head_groups
    rows_in = query_rows.shape[0]
    packed = jnp.concatenate(
        [
            query_rows.reshape(rows_in, head_groups, width_q),
            key_rows.reshape(rows_in, head_groups, width_k),
            value_rows.reshape(rows_in, head_groups, width_k),
            out_grads.reshape(rows_in, head_groups, width_q),
        ],
        axis=2,
    )
    moved = lax.all_to_all(packed, "head", split_axis=1, concat_axis=0, tiled=True)
    moved = moved.reshape(moved.shape[0], moved.shape[2])
    head_query = moved[:, :width_q]
    head_key = moved[:, width_q : width_q + width_k]
    head_value = moved[:, width_q + width_k : width_q + 2 * width_k]
    head_grad = moved[:, width_q + 2 * width_k :]
    row_count = head_query.shape[0]
    tiles_here = row_count // TILE
    kv_width = head_key.shape[1]
    kv_heads = kv_width // HD
    group_size = head_query.shape[1] // kv_width
    scaling = HD ** (-0.5)
    block_index = lax.axis_index("blk")
    first_tile = block_index * tiles_here
    window_first = (block_index - SPAN_DEV) * tiles_here
    window_slots = (SPAN_DEV + 1) * tiles_here
    own_states = jnp.concatenate(
        [
            head_key.reshape(tiles_here, TILE, kv_width),
            head_value.reshape(tiles_here, TILE, kv_width),
        ],
        axis=2,
    )
    my_lists = lax.dynamic_slice_in_dim(ancestors, first_tile, tiles_here, 0)
    prompt_ids = jnp.arange(PROMPT_TILES, dtype=jnp.int32)
    pieces = [tree_spread(own_states[:PROMPT_TILES], "blk")]
    for offset in range(SPAN_DEV, 0, -1):
        pieces.append(passed_along(own_states, "blk", offset))
    pieces.append(own_states)
    table = jnp.concatenate(pieces, axis=0)
    slot_index = jnp.arange(window_slots, dtype=jnp.int32)
    prompt_sum = jnp.zeros((PROMPT_TILES, TILE, 2 * kv_width), jnp.float32)
    near_sum = jnp.zeros((window_slots, TILE * 2 * kv_width), jnp.float32)
    query_parts = []
    for local in range(tiles_here):
        tile_id = first_tile + local
        listed = my_lists[local]
        tile_ids = jnp.concatenate([prompt_ids, listed, tile_id[None]])
        near_rows = jnp.where(listed >= 0, PROMPT_TILES + listed - window_first, 0)
        own_row = jnp.full((1,), PROMPT_TILES + SPAN_DEV * tiles_here + local, jnp.int32)
        table_rows = jnp.concatenate([prompt_ids, near_rows, own_row])
        chosen = jnp.take(table, table_rows, axis=0)
        key_block = chosen[:, :, :kv_width].reshape(KEYT * TILE, kv_heads, HD)
        value_block = chosen[:, :, kv_width:].reshape(KEYT * TILE, kv_heads, HD)
        allowed = visible_mask(tile_id, tile_ids, listed, lengths)
        live_rows = jnp.arange(TILE, dtype=jnp.int32) < lengths[tile_id]
        tile_query = head_query[local * TILE : (local + 1) * TILE].reshape(
            TILE, kv_heads, group_size, HD
        )
        tile_grad = head_grad[local * TILE : (local + 1) * TILE].reshape(
            TILE, kv_heads, group_size, HD
        )
        query_part, key_part, value_part = tile_backward(
            tile_query, tile_grad, key_block, value_block, allowed, live_rows, scaling
        )
        query_parts.append(query_part.reshape(TILE, group_size * kv_width))
        tile_terms = jnp.concatenate(
            [key_part.reshape(KEYT, TILE, kv_width), value_part.reshape(KEYT, TILE, kv_width)],
            axis=2,
        )
        prompt_sum = prompt_sum + tile_terms[:PROMPT_TILES]
        window_ids = jnp.concatenate(
            [listed - window_first, jnp.full((1,), SPAN_DEV * tiles_here + local, jnp.int32)]
        )
        usable = jnp.concatenate([listed >= 0, jnp.ones((1,), bool)])
        placing = ((window_ids[:, None] == slot_index[None, :]) & usable[:, None]).astype(
            jnp.float32
        )
        near_sum = near_sum + jnp.einsum(
            "sw,sx->wx",
            placing,
            tile_terms[PROMPT_TILES:].reshape(ANC + 1, TILE * 2 * kv_width),
            precision=lax.Precision.HIGHEST,
        )
    root_total = tree_total(prompt_sum, "blk")
    near_parts = near_sum.reshape(SPAN_DEV + 1, tiles_here, TILE, 2 * kv_width)
    total = near_parts[SPAN_DEV]
    for offset in range(1, SPAN_DEV + 1):
        total = total + passed_along(near_parts[SPAN_DEV - offset], "blk", -offset)
    total = total.at[:PROMPT_TILES].add(jnp.where(block_index == 0, root_total, 0.0))
    key_out = (total[:, :, :kv_width] * scaling).astype(jnp.bfloat16).reshape(row_count, kv_width)
    value_out = total[:, :, kv_width:].astype(jnp.bfloat16).reshape(row_count, kv_width)
    query_out = jnp.concatenate(query_parts, axis=0)
    joined = jnp.concatenate([query_out, key_out, value_out], axis=1)
    joined = joined.reshape(joined.shape[0], 1, joined.shape[1])
    back = lax.all_to_all(joined, "head", split_axis=0, concat_axis=1, tiled=True)
    rows_out = back.shape[0]
    query_grads = back[:, :, :width_q].reshape(rows_out, head_groups * width_q)
    key_grads = back[:, :, width_q : width_q + width_k].reshape(rows_out, head_groups * width_k)
    value_grads = back[:, :, width_q + width_k :].reshape(rows_out, head_groups * width_k)
    return (query_grads, key_grads, value_grads)


def solution(mesh):
    placed = (
        P(("blk", "head"), None),
        P(("blk", "head"), None),
        P(("blk", "head"), None),
        P(("blk", "head"), None),
        P(),
        P(),
    )
    return jax.shard_map(
        shards,
        mesh=mesh,
        in_specs=placed,
        out_specs=(P(("blk", "head"), None), P(("blk", "head"), None), P(("blk", "head"), None)),
        check_vma=False,
    )
```

```python
import jax
import jax.numpy as jnp
from jax import lax
from jax.sharding import PartitionSpec as P

HD = 128
TILE = 128
SPAN_DEV = 2
PROMPT_TILES = 1
ANC = 5
KEYT = 7


def spread(value, axis, source):
    kept = jnp.where(lax.axis_index(axis) == source, value, 0).astype(value.dtype)
    return lax.psum(kept, axis)


def tree_levels(size):
    levels = []
    stride = 1
    for radix in (2, 4):
        if size % (stride * radix) == 0:
            levels.append((stride, radix))
            stride *= radix
    if size // stride > 1:
        levels.append((stride, size // stride))
    return levels


def tree_spread(value, axis):
    size = lax.axis_size(axis)
    index = lax.axis_index(axis)
    for stride, radix in tree_levels(size):
        got = [
            lax.ppermute(value, axis, [(j, j + k * stride) for j in range(stride)])
            for k in range(1, radix)
        ]
        arrived = got[0]
        for extra in got[1:]:
            arrived = arrived + extra
        value = jnp.where(index < stride, value, arrived)
    return value


def binary_levels(size):
    levels = []
    for stride, radix in tree_levels(size):
        if radix & (radix - 1) == 0:
            while radix > 1:
                levels.append((stride, 2))
                stride *= 2
                radix //= 2
        else:
            levels.append((stride, radix))
    return levels


def tree_total(value, axis):
    size = lax.axis_size(axis)
    for stride, radix in reversed(tree_levels(size)[:-1] + binary_levels(size)[-3:]):
        got = [
            lax.ppermute(value, axis, [(j + k * stride, j) for j in range(stride)])
            for k in range(1, radix)
        ]
        for extra in got:
            value = value + extra
    return value


def gathered_total(value, axis):
    size = lax.axis_size(axis)
    if value.size % size:
        return tree_total(value, axis)
    pieces = value.reshape(size, value.size // size)
    mine = jnp.sum(lax.all_to_all(pieces, axis, 0, 0, tiled=True), axis=0)
    spread_out = jnp.broadcast_to(mine[None], pieces.shape)
    return lax.all_to_all(spread_out, axis, 0, 0, tiled=True).reshape(value.shape)


def passed_along(block, axis, distance):
    devices = range(lax.axis_size(axis))
    route = [(i - distance, i) for i in devices if i - distance in devices]
    return lax.ppermute(block, axis, route)


def visible_mask(tile_id, tile_ids, listed, lengths):
    position = jnp.arange(TILE, dtype=jnp.int32)
    slot_ok = jnp.concatenate(
        [jnp.arange(PROMPT_TILES, dtype=jnp.int32) < tile_id, listed >= 0, jnp.ones((1,), bool)]
    )
    key_len = jnp.take(lengths, jnp.maximum(tile_ids, 0))
    key_ok = slot_ok[:, None] & (position[None, :] < key_len[:, None])
    own_slot = jnp.arange(KEYT) == KEYT - 1
    causal = position[None, None, :] <= position[:, None, None]
    allowed = key_ok[None, :, :] & (causal | ~own_slot[None, :, None])
    return allowed.reshape(TILE, KEYT * TILE)


def tile_backward(queries, grads_out, key_block, value_block, allowed, live_rows, scaling):
    scores = (
        jnp.einsum("igrd,jgd->grij", queries, key_block, preferred_element_type=jnp.float32)
        * scaling
    )
    scores = jnp.where(allowed, scores, -jnp.inf)
    row_max = jnp.max(scores, axis=-1, keepdims=True)
    log_total = row_max + jnp.log(jnp.sum(jnp.exp(scores - row_max), axis=-1, keepdims=True))
    weights = jnp.where(allowed & live_rows[:, None], jnp.exp(scores - log_total), 0.0)
    weight_grads = jnp.einsum(
        "igrd,jgd->grij", grads_out, value_block, preferred_element_type=jnp.float32
    )
    row_dot = jnp.sum(weights * weight_grads, axis=-1, keepdims=True)
    score_grads = (weights * (weight_grads - row_dot)).astype(jnp.bfloat16)
    weights_low = weights.astype(jnp.bfloat16)
    query_part = (
        jnp.einsum("grij,jgd->igrd", score_grads, key_block, preferred_element_type=jnp.float32)
        * scaling
    )
    key_part = jnp.einsum(
        "grij,igrd->jgd", score_grads, queries, preferred_element_type=jnp.float32
    )
    value_part = jnp.einsum(
        "grij,igrd->jgd", weights_low, grads_out, preferred_element_type=jnp.float32
    )
    return (query_part.astype(jnp.bfloat16), key_part, value_part)


def shards(query_rows, key_rows, value_rows, out_grads, lengths, ancestors):
    head_groups = lax.axis_size("head")
    width_q = query_rows.shape[1] // head_groups
    width_k = key_rows.shape[1] // head_groups
    rows_in = query_rows.shape[0]
    packed = jnp.concatenate(
        [
            query_rows.reshape(rows_in, head_groups, width_q),
            key_rows.reshape(rows_in, head_groups, width_k),
            value_rows.reshape(rows_in, head_groups, width_k),
            out_grads.reshape(rows_in, head_groups, width_q),
        ],
        axis=2,
    )
    moved = lax.all_to_all(packed, "head", split_axis=1, concat_axis=0, tiled=True)
    moved = moved.reshape(moved.shape[0], moved.shape[2])
    head_query = moved[:, :width_q]
    head_key = moved[:, width_q : width_q + width_k]
    head_value = moved[:, width_q + width_k : width_q + 2 * width_k]
    head_grad = moved[:, width_q + 2 * width_k :]
    row_count = head_query.shape[0]
    tiles_here = row_count // TILE
    kv_width = head_key.shape[1]
    kv_heads = kv_width // HD
    group_size = head_query.shape[1] // kv_width
    scaling = HD ** (-0.5)
    block_index = lax.axis_index("blk")
    first_tile = block_index * tiles_here
    window_first = (block_index - SPAN_DEV) * tiles_here
    window_slots = (SPAN_DEV + 1) * tiles_here
    own_states = jnp.concatenate(
        [
            head_key.reshape(tiles_here, TILE, kv_width),
            head_value.reshape(tiles_here, TILE, kv_width),
        ],
        axis=2,
    )
    my_lists = lax.dynamic_slice_in_dim(ancestors, first_tile, tiles_here, 0)
    prompt_ids = jnp.arange(PROMPT_TILES, dtype=jnp.int32)
    pieces = [tree_spread(own_states[:PROMPT_TILES], "blk")]
    for offset in range(SPAN_DEV, 0, -1):
        pieces.append(passed_along(own_states, "blk", offset))
    pieces.append(own_states)
    table = jnp.concatenate(pieces, axis=0)
    slot_index = jnp.arange(window_slots, dtype=jnp.int32)
    prompt_sum = jnp.zeros((PROMPT_TILES, TILE, 2 * kv_width), jnp.float32)
    near_sum = jnp.zeros((window_slots, TILE * 2 * kv_width), jnp.float32)
    query_parts = []
    for local in range(tiles_here):
        tile_id = first_tile + local
        listed = my_lists[local]
        tile_ids = jnp.concatenate([prompt_ids, listed, tile_id[None]])
        near_rows = jnp.where(listed >= 0, PROMPT_TILES + listed - window_first, 0)
        own_row = jnp.full((1,), PROMPT_TILES + SPAN_DEV * tiles_here + local, jnp.int32)
        table_rows = jnp.concatenate([prompt_ids, near_rows, own_row])
        chosen = jnp.take(table, table_rows, axis=0)
        key_block = chosen[:, :, :kv_width].reshape(KEYT * TILE, kv_heads, HD)
        value_block = chosen[:, :, kv_width:].reshape(KEYT * TILE, kv_heads, HD)
        allowed = visible_mask(tile_id, tile_ids, listed, lengths)
        live_rows = jnp.arange(TILE, dtype=jnp.int32) < lengths[tile_id]
        tile_query = head_query[local * TILE : (local + 1) * TILE].reshape(
            TILE, kv_heads, group_size, HD
        )
        tile_grad = head_grad[local * TILE : (local + 1) * TILE].reshape(
            TILE, kv_heads, group_size, HD
        )
        query_part, key_part, value_part = tile_backward(
            tile_query, tile_grad, key_block, value_block, allowed, live_rows, scaling
        )
        query_parts.append(query_part.reshape(TILE, group_size * kv_width))
        tile_terms = jnp.concatenate(
            [key_part.reshape(KEYT, TILE, kv_width), value_part.reshape(KEYT, TILE, kv_width)],
            axis=2,
        )
        prompt_sum = prompt_sum + tile_terms[:PROMPT_TILES]
        window_ids = jnp.concatenate(
            [listed - window_first, jnp.full((1,), SPAN_DEV * tiles_here + local, jnp.int32)]
        )
        usable = jnp.concatenate([listed >= 0, jnp.ones((1,), bool)])
        placing = ((window_ids[:, None] == slot_index[None, :]) & usable[:, None]).astype(
            jnp.float32
        )
        near_sum = near_sum + jnp.einsum(
            "sw,sx->wx",
            placing,
            tile_terms[PROMPT_TILES:].reshape(ANC + 1, TILE * 2 * kv_width),
            precision=lax.Precision.HIGHEST,
        )
    root_total = gathered_total(prompt_sum, "blk")
    near_parts = near_sum.reshape(SPAN_DEV + 1, tiles_here, TILE, 2 * kv_width)
    total = near_parts[SPAN_DEV]
    for offset in range(1, SPAN_DEV + 1):
        total = total + passed_along(near_parts[SPAN_DEV - offset], "blk", -offset)
    total = total.at[:PROMPT_TILES].add(jnp.where(block_index == 0, root_total, 0.0))
    key_out = (total[:, :, :kv_width] * scaling).astype(jnp.bfloat16).reshape(row_count, kv_width)
    value_out = total[:, :, kv_width:].astype(jnp.bfloat16).reshape(row_count, kv_width)
    query_out = jnp.concatenate(query_parts, axis=0)
    joined = jnp.concatenate([query_out, key_out, value_out], axis=1)
    joined = joined.reshape(joined.shape[0], 1, joined.shape[1])
    back = lax.all_to_all(joined, "head", split_axis=0, concat_axis=1, tiled=True)
    rows_out = back.shape[0]
    query_grads = back[:, :, :width_q].reshape(rows_out, head_groups * width_q)
    key_grads = back[:, :, width_q : width_q + width_k].reshape(rows_out, head_groups * width_k)
    value_grads = back[:, :, width_q + width_k :].reshape(rows_out, head_groups * width_k)
    return (query_grads, key_grads, value_grads)


def solution(mesh):
    placed = (
        P(("blk", "head"), None),
        P(("blk", "head"), None),
        P(("blk", "head"), None),
        P(("blk", "head"), None),
        P(),
        P(),
    )
    return jax.shard_map(
        shards,
        mesh=mesh,
        in_specs=placed,
        out_specs=(P(("blk", "head"), None), P(("blk", "head"), None), P(("blk", "head"), None)),
        check_vma=False,
    )
```

```python
import jax
import jax.numpy as jnp
from jax import lax
from jax.sharding import PartitionSpec as P
from jax.experimental import pallas as pl
from jax.experimental.pallas import tpu as pltpu

HD = 128
TILE = 128
SPAN_DEV = 2
PROMPT_TILES = 1
ANC = 5
KEYT = 7


def spread(value, axis, source):
    kept = jnp.where(lax.axis_index(axis) == source, value, 0).astype(value.dtype)
    return lax.psum(kept, axis)


def tree_levels(size):
    levels = []
    stride = 1
    for radix in (2, 4):
        if size % (stride * radix) == 0:
            levels.append((stride, radix))
            stride *= radix
    if size // stride > 1:
        levels.append((stride, size // stride))
    return levels


def tree_spread(value, axis):
    size = lax.axis_size(axis)
    index = lax.axis_index(axis)
    for stride, radix in tree_levels(size):
        got = [
            lax.ppermute(value, axis, [(j, j + k * stride) for j in range(stride)])
            for k in range(1, radix)
        ]
        arrived = got[0]
        for extra in got[1:]:
            arrived = arrived + extra
        value = jnp.where(index < stride, value, arrived)
    return value


def binary_levels(size):
    levels = []
    for stride, radix in tree_levels(size):
        if radix & (radix - 1) == 0:
            while radix > 1:
                levels.append((stride, 2))
                stride *= 2
                radix //= 2
        else:
            levels.append((stride, radix))
    return levels


def tree_total(value, axis):
    size = lax.axis_size(axis)
    for stride, radix in reversed(tree_levels(size)[:-1] + binary_levels(size)[-3:]):
        got = [
            lax.ppermute(value, axis, [(j + k * stride, j) for j in range(stride)])
            for k in range(1, radix)
        ]
        for extra in got:
            value = value + extra
    return value


def passed_along(block, axis, distance):
    devices = range(lax.axis_size(axis))
    route = [(i - distance, i) for i in devices if i - distance in devices]
    return lax.ppermute(block, axis, route)


def visible_mask(tile_id, tile_ids, listed, lengths):
    position = jnp.arange(TILE, dtype=jnp.int32)
    slot_ok = jnp.concatenate(
        [jnp.arange(PROMPT_TILES, dtype=jnp.int32) < tile_id, listed >= 0, jnp.ones((1,), bool)]
    )
    key_len = jnp.take(lengths, jnp.maximum(tile_ids, 0))
    key_ok = slot_ok[:, None] & (position[None, :] < key_len[:, None])
    own_slot = jnp.arange(KEYT) == KEYT - 1
    causal = position[None, None, :] <= position[:, None, None]
    allowed = key_ok[None, :, :] & (causal | ~own_slot[None, :, None])
    return allowed.reshape(TILE, KEYT * TILE)


def tile_backward(queries, grads_out, key_block, value_block, allowed, live_rows, scaling):
    scores = (
        jnp.einsum("igrd,jgd->grij", queries, key_block, preferred_element_type=jnp.float32)
        * scaling
    )
    scores = jnp.where(allowed, scores, -jnp.inf)
    row_max = jnp.max(scores, axis=-1, keepdims=True)
    log_total = row_max + jnp.log(jnp.sum(jnp.exp(scores - row_max), axis=-1, keepdims=True))
    weights = jnp.where(allowed & live_rows[:, None], jnp.exp(scores - log_total), 0.0)
    weight_grads = jnp.einsum(
        "igrd,jgd->grij", grads_out, value_block, preferred_element_type=jnp.float32
    )
    row_dot = jnp.sum(weights * weight_grads, axis=-1, keepdims=True)
    score_grads = (weights * (weight_grads - row_dot)).astype(jnp.bfloat16)
    weights_low = weights.astype(jnp.bfloat16)
    query_part = (
        jnp.einsum("grij,jgd->igrd", score_grads, key_block, preferred_element_type=jnp.float32)
        * scaling
    )
    key_part = jnp.einsum(
        "grij,igrd->jgd", score_grads, queries, preferred_element_type=jnp.float32
    )
    value_part = jnp.einsum(
        "grij,igrd->jgd", weights_low, grads_out, preferred_element_type=jnp.float32
    )
    return (query_part.astype(jnp.bfloat16), key_part, value_part)


def tiles_kernel(q_ref, g_ref, k_ref, v_ref, pos_ref, live_ref, dq_ref, dk_ref, dv_ref, *, group, scaling):
    keys = k_ref[0]
    values = v_ref[0]
    rows = lax.broadcasted_iota(jnp.int32, (q_ref.shape[0], keys.shape[0]), 0)
    seen = pos_ref[0] <= rows
    kept = seen & (live_ref[0] > 0)
    dk_acc = jnp.zeros(dk_ref.shape[1:], jnp.float32)
    dv_acc = jnp.zeros(dv_ref.shape[1:], jnp.float32)
    width = keys.shape[1]
    for r in range(group):
        cols = slice(r * width, (r + 1) * width)
        qr = q_ref[:, cols]
        gr = g_ref[:, cols]
        scores = lax.dot_general(qr, keys, (((1,), (1,)), ((), ())), preferred_element_type=jnp.float32)
        scores = jnp.where(seen, scores * scaling, -jnp.inf)
        row_max = jnp.max(scores, axis=1, keepdims=True)
        log_total = row_max + jnp.log(jnp.sum(jnp.exp(scores - row_max), axis=1, keepdims=True))
        weights = jnp.where(kept, jnp.exp(scores - log_total), 0.0)
        weight_grads = lax.dot_general(gr, values, (((1,), (1,)), ((), ())), preferred_element_type=jnp.float32)
        row_dot = jnp.sum(weights * weight_grads, axis=1, keepdims=True)
        score_grads = (weights * (weight_grads - row_dot)).astype(jnp.bfloat16)
        weights_low = weights.astype(jnp.bfloat16)
        dq = jnp.dot(score_grads, keys, preferred_element_type=jnp.float32) * scaling
        dq_ref[:, cols] = dq.astype(dq_ref.dtype)
        dk_acc = dk_acc + lax.dot_general(score_grads, qr, (((0,), (0,)), ((), ())), preferred_element_type=jnp.float32)
        dv_acc = dv_acc + lax.dot_general(weights_low, gr, (((0,), (0,)), ((), ())), preferred_element_type=jnp.float32)
    dk_ref[0] = dk_acc
    dv_ref[0] = dv_acc


def tiles_backward(queries, grads_out, keys, values, positions, live, scaling, interpret=False):
    tiles, key_slots, width = keys.shape
    group = queries.shape[1] // width
    rows = queries.shape[0] // tiles
    row_spec = pl.BlockSpec((rows, queries.shape[1]), lambda t: (t, 0))
    key_spec = pl.BlockSpec((1, key_slots, width), lambda t: (t, 0, 0))
    kernel = lambda *refs: tiles_kernel(*refs, group=group, scaling=scaling)
    return pl.pallas_call(
        kernel,
        grid=(tiles,),
        in_specs=[
            row_spec,
            row_spec,
            key_spec,
            key_spec,
            pl.BlockSpec((1, 1, key_slots), lambda t: (t, 0, 0)),
            pl.BlockSpec((1, rows, 1), lambda t: (t, 0, 0)),
        ],
        out_specs=[row_spec, key_spec, key_spec],
        out_shape=[
            jax.ShapeDtypeStruct(queries.shape, jnp.bfloat16),
            jax.ShapeDtypeStruct(keys.shape, jnp.float32),
            jax.ShapeDtypeStruct(keys.shape, jnp.float32),
        ],
        interpret=interpret,
    )(queries, grads_out, keys, values, positions, live)


def column_limits(tile_id, tile_ids, listed, lengths):
    position = jnp.arange(TILE, dtype=jnp.int32)
    slot_ok = jnp.concatenate(
        [jnp.arange(PROMPT_TILES, dtype=jnp.int32) < tile_id, listed >= 0, jnp.ones((1,), bool)]
    )
    key_len = jnp.take(lengths, jnp.maximum(tile_ids, 0))
    key_ok = slot_ok[:, None] & (position[None, :] < key_len[:, None])
    own_slot = (jnp.arange(KEYT) == KEYT - 1)[:, None]
    limit = jnp.where(key_ok, jnp.where(own_slot, position[None, :], 0), TILE)
    return limit.reshape(1, KEYT * TILE)


def shards(query_rows, key_rows, value_rows, out_grads, lengths, ancestors):
    head_groups = lax.axis_size("head")
    width_q = query_rows.shape[1] // head_groups
    width_k = key_rows.shape[1] // head_groups
    rows_in = query_rows.shape[0]
    packed = jnp.concatenate(
        [
            query_rows.reshape(rows_in, head_groups, width_q),
            key_rows.reshape(rows_in, head_groups, width_k),
            value_rows.reshape(rows_in, head_groups, width_k),
            out_grads.reshape(rows_in, head_groups, width_q),
        ],
        axis=2,
    )
    moved = lax.all_to_all(packed, "head", split_axis=1, concat_axis=0, tiled=True)
    moved = moved.reshape(moved.shape[0], moved.shape[2])
    head_query = moved[:, :width_q]
    head_key = moved[:, width_q : width_q + width_k]
    head_value = moved[:, width_q + width_k : width_q + 2 * width_k]
    head_grad = moved[:, width_q + 2 * width_k :]
    row_count = head_query.shape[0]
    tiles_here = row_count // TILE
    kv_width = head_key.shape[1]
    kv_heads = kv_width // HD
    group_size = head_query.shape[1] // kv_width
    scaling = HD ** (-0.5)
    block_index = lax.axis_index("blk")
    first_tile = block_index * tiles_here
    window_first = (block_index - SPAN_DEV) * tiles_here
    window_slots = (SPAN_DEV + 1) * tiles_here
    own_states = jnp.concatenate(
        [
            head_key.reshape(tiles_here, TILE, kv_width),
            head_value.reshape(tiles_here, TILE, kv_width),
        ],
        axis=2,
    )
    my_lists = lax.dynamic_slice_in_dim(ancestors, first_tile, tiles_here, 0)
    prompt_ids = jnp.arange(PROMPT_TILES, dtype=jnp.int32)
    pieces = [tree_spread(own_states[:PROMPT_TILES], "blk")]
    for offset in range(SPAN_DEV, 0, -1):
        pieces.append(passed_along(own_states, "blk", offset))
    pieces.append(own_states)
    table = jnp.concatenate(pieces, axis=0)
    slot_index = jnp.arange(window_slots, dtype=jnp.int32)
    prompt_sum = jnp.zeros((PROMPT_TILES, TILE, 2 * kv_width), jnp.float32)
    near_sum = jnp.zeros((window_slots, TILE * 2 * kv_width), jnp.float32)
    key_blocks, value_blocks, limits, lives, window_rows = [], [], [], [], []
    for local in range(tiles_here):
        tile_id = first_tile + local
        listed = my_lists[local]
        tile_ids = jnp.concatenate([prompt_ids, listed, tile_id[None]])
        near_rows = jnp.where(listed >= 0, PROMPT_TILES + listed - window_first, 0)
        own_row = jnp.full((1,), PROMPT_TILES + SPAN_DEV * tiles_here + local, jnp.int32)
        table_rows = jnp.concatenate([prompt_ids, near_rows, own_row])
        chosen = jnp.take(table, table_rows, axis=0)
        key_blocks.append(chosen[:, :, :kv_width].reshape(KEYT * TILE, kv_width))
        value_blocks.append(chosen[:, :, kv_width:].reshape(KEYT * TILE, kv_width))
        limits.append(column_limits(tile_id, tile_ids, listed, lengths))
        lives.append((jnp.arange(TILE, dtype=jnp.int32) < lengths[tile_id]).astype(jnp.int32)[:, None])
        window_rows.append(listed)
    query_out, key_parts, value_parts = tiles_backward(
        head_query,
        head_grad,
        jnp.stack(key_blocks),
        jnp.stack(value_blocks),
        jnp.stack(limits),
        jnp.stack(lives),
        scaling,
    )
    for local in range(tiles_here):
        listed = window_rows[local]
        tile_terms = jnp.concatenate(
            [
                key_parts[local].reshape(KEYT, TILE, kv_width),
                value_parts[local].reshape(KEYT, TILE, kv_width),
            ],
            axis=2,
        )
        prompt_sum = prompt_sum + tile_terms[:PROMPT_TILES]
        window_ids = jnp.concatenate(
            [listed - window_first, jnp.full((1,), SPAN_DEV * tiles_here + local, jnp.int32)]
        )
        usable = jnp.concatenate([listed >= 0, jnp.ones((1,), bool)])
        placing = ((window_ids[:, None] == slot_index[None, :]) & usable[:, None]).astype(
            jnp.float32
        )
        near_sum = near_sum + jnp.einsum(
            "sw,sx->wx",
            placing,
            tile_terms[PROMPT_TILES:].reshape(ANC + 1, TILE * 2 * kv_width),
            precision=lax.Precision.HIGHEST,
        )
    root_total = tree_total(prompt_sum, "blk")
    near_parts = near_sum.reshape(SPAN_DEV + 1, tiles_here, TILE, 2 * kv_width)
    total = near_parts[SPAN_DEV]
    for offset in range(1, SPAN_DEV + 1):
        total = total + passed_along(near_parts[SPAN_DEV - offset], "blk", -offset)
    total = total.at[:PROMPT_TILES].add(jnp.where(block_index == 0, root_total, 0.0))
    key_out = (total[:, :, :kv_width] * scaling).astype(jnp.bfloat16).reshape(row_count, kv_width)
    value_out = total[:, :, kv_width:].astype(jnp.bfloat16).reshape(row_count, kv_width)
    joined = jnp.concatenate([query_out, key_out, value_out], axis=1)
    joined = joined.reshape(joined.shape[0], 1, joined.shape[1])
    back = lax.all_to_all(joined, "head", split_axis=0, concat_axis=1, tiled=True)
    rows_out = back.shape[0]
    query_grads = back[:, :, :width_q].reshape(rows_out, head_groups * width_q)
    key_grads = back[:, :, width_q : width_q + width_k].reshape(rows_out, head_groups * width_k)
    value_grads = back[:, :, width_q + width_k :].reshape(rows_out, head_groups * width_k)
    return (query_grads, key_grads, value_grads)


def solution(mesh):
    placed = (
        P(("blk", "head"), None),
        P(("blk", "head"), None),
        P(("blk", "head"), None),
        P(("blk", "head"), None),
        P(),
        P(),
    )
    return jax.shard_map(
        shards,
        mesh=mesh,
        in_specs=placed,
        out_specs=(P(("blk", "head"), None), P(("blk", "head"), None), P(("blk", "head"), None)),
        check_vma=False,
    )
```

```python
import jax
import jax.numpy as jnp
from jax import lax
from jax.sharding import PartitionSpec as P
from jax.experimental import pallas as pl
from jax.experimental.pallas import tpu as pltpu

HD = 128
TILE = 128
SPAN_DEV = 2
PROMPT_TILES = 1
ANC = 5
KEYT = 7


def spread(value, axis, source):
    kept = jnp.where(lax.axis_index(axis) == source, value, 0).astype(value.dtype)
    return lax.psum(kept, axis)


def tree_levels(size):
    levels = []
    stride = 1
    for radix in (2, 4):
        if size % (stride * radix) == 0:
            levels.append((stride, radix))
            stride *= radix
    if size // stride > 1:
        levels.append((stride, size // stride))
    return levels


def tree_spread(value, axis):
    size = lax.axis_size(axis)
    index = lax.axis_index(axis)
    for stride, radix in spread_levels(size):
        got = [
            lax.ppermute(value, axis, [(j, j + k * stride) for j in range(stride)])
            for k in range(1, radix)
        ]
        arrived = got[0]
        for extra in got[1:]:
            arrived = arrived + extra
        value = jnp.where(index < stride, value, arrived)
    return value


def binary_levels(size):
    levels = []
    for stride, radix in tree_levels(size):
        if radix & (radix - 1) == 0:
            while radix > 1:
                levels.append((stride, 2))
                stride *= 2
                radix //= 2
        else:
            levels.append((stride, radix))
    return levels


def spread_levels(size):
    levels = tree_levels(size)
    stride, radix = levels[-1]
    if radix > 4 and radix % 4 == 0:
        levels = levels[:-1] + [(stride, 4), (stride * 4, radix // 4)]
    return levels


def total_levels(size):
    levels = tree_levels(size)
    if len(levels) < 2:
        return levels
    inner = levels[-1][0]
    return [(1, inner), (inner, size // inner)]


def tree_total(value, axis):
    size = lax.axis_size(axis)
    for stride, radix in reversed(total_levels(size)):
        got = [
            lax.ppermute(value, axis, [(j + k * stride, j) for j in range(stride)])
            for k in range(1, radix)
        ]
        for extra in got:
            value = value + extra
    return value


def passed_along(block, axis, distance):
    devices = range(lax.axis_size(axis))
    route = [(i - distance, i) for i in devices if i - distance in devices]
    return lax.ppermute(block, axis, route)


def visible_mask(tile_id, tile_ids, listed, lengths):
    position = jnp.arange(TILE, dtype=jnp.int32)
    slot_ok = jnp.concatenate(
        [jnp.arange(PROMPT_TILES, dtype=jnp.int32) < tile_id, listed >= 0, jnp.ones((1,), bool)]
    )
    key_len = jnp.take(lengths, jnp.maximum(tile_ids, 0))
    key_ok = slot_ok[:, None] & (position[None, :] < key_len[:, None])
    own_slot = jnp.arange(KEYT) == KEYT - 1
    causal = position[None, None, :] <= position[:, None, None]
    allowed = key_ok[None, :, :] & (causal | ~own_slot[None, :, None])
    return allowed.reshape(TILE, KEYT * TILE)


def tile_backward(queries, grads_out, key_block, value_block, allowed, live_rows, scaling):
    scores = (
        jnp.einsum("igrd,jgd->grij", queries, key_block, preferred_element_type=jnp.float32)
        * scaling
    )
    scores = jnp.where(allowed, scores, -jnp.inf)
    row_max = jnp.max(scores, axis=-1, keepdims=True)
    log_total = row_max + jnp.log(jnp.sum(jnp.exp(scores - row_max), axis=-1, keepdims=True))
    weights = jnp.where(allowed & live_rows[:, None], jnp.exp(scores - log_total), 0.0)
    weight_grads = jnp.einsum(
        "igrd,jgd->grij", grads_out, value_block, preferred_element_type=jnp.float32
    )
    row_dot = jnp.sum(weights * weight_grads, axis=-1, keepdims=True)
    score_grads = (weights * (weight_grads - row_dot)).astype(jnp.bfloat16)
    weights_low = weights.astype(jnp.bfloat16)
    query_part = (
        jnp.einsum("grij,jgd->igrd", score_grads, key_block, preferred_element_type=jnp.float32)
        * scaling
    )
    key_part = jnp.einsum(
        "grij,igrd->jgd", score_grads, queries, preferred_element_type=jnp.float32
    )
    value_part = jnp.einsum(
        "grij,igrd->jgd", weights_low, grads_out, preferred_element_type=jnp.float32
    )
    return (query_part.astype(jnp.bfloat16), key_part, value_part)


def tiles_kernel(q_ref, g_ref, k_ref, v_ref, pos_ref, live_ref, dq_ref, dk_ref, dv_ref, *, group, scaling):
    keys = k_ref[0]
    values = v_ref[0]
    rows = lax.broadcasted_iota(jnp.int32, (q_ref.shape[0], keys.shape[0]), 0)
    seen = pos_ref[0] <= rows
    kept = seen & (live_ref[0] > 0)
    dk_acc = jnp.zeros(dk_ref.shape[1:], jnp.float32)
    dv_acc = jnp.zeros(dv_ref.shape[1:], jnp.float32)
    width = keys.shape[1]
    for r in range(group):
        cols = slice(r * width, (r + 1) * width)
        qr = q_ref[:, cols]
        gr = g_ref[:, cols]
        scores = lax.dot_general(qr, keys, (((1,), (1,)), ((), ())), preferred_element_type=jnp.float32)
        scores = jnp.where(seen, scores * scaling, -jnp.inf)
        row_max = jnp.max(scores, axis=1, keepdims=True)
        log_total = row_max + jnp.log(jnp.sum(jnp.exp(scores - row_max), axis=1, keepdims=True))
        weights = jnp.where(kept, jnp.exp(scores - log_total), 0.0)
        weight_grads = lax.dot_general(gr, values, (((1,), (1,)), ((), ())), preferred_element_type=jnp.float32)
        row_dot = jnp.sum(weights * weight_grads, axis=1, keepdims=True)
        score_grads = (weights * (weight_grads - row_dot)).astype(jnp.bfloat16)
        weights_low = weights.astype(jnp.bfloat16)
        dq = jnp.dot(score_grads, keys, preferred_element_type=jnp.float32) * scaling
        dq_ref[:, cols] = dq.astype(dq_ref.dtype)
        dk_acc = dk_acc + lax.dot_general(score_grads, qr, (((0,), (0,)), ((), ())), preferred_element_type=jnp.float32)
        dv_acc = dv_acc + lax.dot_general(weights_low, gr, (((0,), (0,)), ((), ())), preferred_element_type=jnp.float32)
    dk_ref[0] = dk_acc
    dv_ref[0] = dv_acc


def tiles_backward(queries, grads_out, keys, values, positions, live, scaling, interpret=False):
    tiles, key_slots, width = keys.shape
    group = queries.shape[1] // width
    rows = queries.shape[0] // tiles
    row_spec = pl.BlockSpec((rows, queries.shape[1]), lambda t: (t, 0))
    key_spec = pl.BlockSpec((1, key_slots, width), lambda t: (t, 0, 0))
    kernel = lambda *refs: tiles_kernel(*refs, group=group, scaling=scaling)
    return pl.pallas_call(
        kernel,
        grid=(tiles,),
        in_specs=[
            row_spec,
            row_spec,
            key_spec,
            key_spec,
            pl.BlockSpec((1, 1, key_slots), lambda t: (t, 0, 0)),
            pl.BlockSpec((1, rows, 1), lambda t: (t, 0, 0)),
        ],
        out_specs=[row_spec, key_spec, key_spec],
        out_shape=[
            jax.ShapeDtypeStruct(queries.shape, jnp.bfloat16),
            jax.ShapeDtypeStruct(keys.shape, jnp.float32),
            jax.ShapeDtypeStruct(keys.shape, jnp.float32),
        ],
        interpret=interpret,
    )(queries, grads_out, keys, values, positions, live)


def column_limits(tile_id, tile_ids, listed, lengths):
    position = jnp.arange(TILE, dtype=jnp.int32)
    slot_ok = jnp.concatenate(
        [jnp.arange(PROMPT_TILES, dtype=jnp.int32) < tile_id, listed >= 0, jnp.ones((1,), bool)]
    )
    key_len = jnp.take(lengths, jnp.maximum(tile_ids, 0))
    key_ok = slot_ok[:, None] & (position[None, :] < key_len[:, None])
    own_slot = (jnp.arange(KEYT) == KEYT - 1)[:, None]
    limit = jnp.where(key_ok, jnp.where(own_slot, position[None, :], 0), TILE)
    return limit.reshape(1, KEYT * TILE)


def shards(query_rows, key_rows, value_rows, out_grads, lengths, ancestors):
    head_groups = lax.axis_size("head")
    width_q = query_rows.shape[1] // head_groups
    width_k = key_rows.shape[1] // head_groups
    rows_in = query_rows.shape[0]
    packed = jnp.concatenate(
        [
            query_rows.reshape(rows_in, head_groups, width_q),
            key_rows.reshape(rows_in, head_groups, width_k),
            value_rows.reshape(rows_in, head_groups, width_k),
            out_grads.reshape(rows_in, head_groups, width_q),
        ],
        axis=2,
    )
    moved = lax.all_to_all(packed, "head", split_axis=1, concat_axis=0, tiled=True)
    moved = moved.reshape(moved.shape[0], moved.shape[2])
    head_query = moved[:, :width_q]
    head_key = moved[:, width_q : width_q + width_k]
    head_value = moved[:, width_q + width_k : width_q + 2 * width_k]
    head_grad = moved[:, width_q + 2 * width_k :]
    row_count = head_query.shape[0]
    tiles_here = row_count // TILE
    kv_width = head_key.shape[1]
    kv_heads = kv_width // HD
    group_size = head_query.shape[1] // kv_width
    scaling = HD ** (-0.5)
    block_index = lax.axis_index("blk")
    first_tile = block_index * tiles_here
    window_first = (block_index - SPAN_DEV) * tiles_here
    window_slots = (SPAN_DEV + 1) * tiles_here
    own_states = jnp.concatenate(
        [
            head_key.reshape(tiles_here, TILE, kv_width),
            head_value.reshape(tiles_here, TILE, kv_width),
        ],
        axis=2,
    )
    my_lists = lax.dynamic_slice_in_dim(ancestors, first_tile, tiles_here, 0)
    prompt_ids = jnp.arange(PROMPT_TILES, dtype=jnp.int32)
    pieces = [tree_spread(own_states[:PROMPT_TILES], "blk")]
    for offset in range(SPAN_DEV, 0, -1):
        pieces.append(passed_along(own_states, "blk", offset))
    pieces.append(own_states)
    table = jnp.concatenate(pieces, axis=0)
    slot_index = jnp.arange(window_slots, dtype=jnp.int32)
    prompt_sum = jnp.zeros((PROMPT_TILES, TILE, 2 * kv_width), jnp.float32)
    near_sum = jnp.zeros((window_slots, TILE * 2 * kv_width), jnp.float32)
    key_blocks, value_blocks, limits, lives, window_rows = [], [], [], [], []
    for local in range(tiles_here):
        tile_id = first_tile + local
        listed = my_lists[local]
        tile_ids = jnp.concatenate([prompt_ids, listed, tile_id[None]])
        near_rows = jnp.where(listed >= 0, PROMPT_TILES + listed - window_first, 0)
        own_row = jnp.full((1,), PROMPT_TILES + SPAN_DEV * tiles_here + local, jnp.int32)
        table_rows = jnp.concatenate([prompt_ids, near_rows, own_row])
        chosen = jnp.take(table, table_rows, axis=0)
        key_blocks.append(chosen[:, :, :kv_width].reshape(KEYT * TILE, kv_width))
        value_blocks.append(chosen[:, :, kv_width:].reshape(KEYT * TILE, kv_width))
        limits.append(column_limits(tile_id, tile_ids, listed, lengths))
        lives.append((jnp.arange(TILE, dtype=jnp.int32) < lengths[tile_id]).astype(jnp.int32)[:, None])
        window_rows.append(listed)
    query_out, key_parts, value_parts = tiles_backward(
        head_query,
        head_grad,
        jnp.stack(key_blocks),
        jnp.stack(value_blocks),
        jnp.stack(limits),
        jnp.stack(lives),
        scaling,
    )
    for local in range(tiles_here):
        listed = window_rows[local]
        tile_terms = jnp.concatenate(
            [
                key_parts[local].reshape(KEYT, TILE, kv_width),
                value_parts[local].reshape(KEYT, TILE, kv_width),
            ],
            axis=2,
        )
        prompt_sum = prompt_sum + tile_terms[:PROMPT_TILES]
        window_ids = jnp.concatenate(
            [listed - window_first, jnp.full((1,), SPAN_DEV * tiles_here + local, jnp.int32)]
        )
        usable = jnp.concatenate([listed >= 0, jnp.ones((1,), bool)])
        placing = ((window_ids[:, None] == slot_index[None, :]) & usable[:, None]).astype(
            jnp.float32
        )
        near_sum = near_sum + jnp.einsum(
            "sw,sx->wx",
            placing,
            tile_terms[PROMPT_TILES:].reshape(ANC + 1, TILE * 2 * kv_width),
            precision=lax.Precision.HIGHEST,
        )
    root_total = tree_total(prompt_sum, "blk")
    near_parts = near_sum.reshape(SPAN_DEV + 1, tiles_here, TILE, 2 * kv_width)
    total = near_parts[SPAN_DEV]
    for offset in range(1, SPAN_DEV + 1):
        total = total + passed_along(near_parts[SPAN_DEV - offset], "blk", -offset)
    total = total.at[:PROMPT_TILES].add(jnp.where(block_index == 0, root_total, 0.0))
    key_out = (total[:, :, :kv_width] * scaling).astype(jnp.bfloat16).reshape(row_count, kv_width)
    value_out = total[:, :, kv_width:].astype(jnp.bfloat16).reshape(row_count, kv_width)
    joined = jnp.concatenate([query_out, key_out, value_out], axis=1)
    joined = joined.reshape(joined.shape[0], 1, joined.shape[1])
    back = lax.all_to_all(joined, "head", split_axis=0, concat_axis=1, tiled=True)
    rows_out = back.shape[0]
    query_grads = back[:, :, :width_q].reshape(rows_out, head_groups * width_q)
    key_grads = back[:, :, width_q : width_q + width_k].reshape(rows_out, head_groups * width_k)
    value_grads = back[:, :, width_q + width_k :].reshape(rows_out, head_groups * width_k)
    return (query_grads, key_grads, value_grads)


def solution(mesh):
    placed = (
        P(("blk", "head"), None),
        P(("blk", "head"), None),
        P(("blk", "head"), None),
        P(("blk", "head"), None),
        P(),
        P(),
    )
    return jax.shard_map(
        shards,
        mesh=mesh,
        in_specs=placed,
        out_specs=(P(("blk", "head"), None), P(("blk", "head"), None), P(("blk", "head"), None)),
        check_vma=False,
    )
```

```python
import jax
import jax.numpy as jnp
from jax import lax
from jax.sharding import PartitionSpec as P
from jax.experimental import pallas as pl
from jax.experimental.pallas import tpu as pltpu

HD = 128
TILE = 128
SPAN_DEV = 2
PROMPT_TILES = 1
ANC = 5
KEYT = 7


def spread(value, axis, source):
    kept = jnp.where(lax.axis_index(axis) == source, value, 0).astype(value.dtype)
    return lax.psum(kept, axis)


def tree_levels(size):
    levels = []
    stride = 1
    for radix in (2, 4):
        if size % (stride * radix) == 0:
            levels.append((stride, radix))
            stride *= radix
    if size // stride > 1:
        levels.append((stride, size // stride))
    return levels


def tree_spread(value, axis):
    size = lax.axis_size(axis)
    index = lax.axis_index(axis)
    for stride, radix in spread_levels(size):
        got = [
            lax.ppermute(value, axis, [(j, j + k * stride) for j in range(stride)])
            for k in range(1, radix)
        ]
        arrived = got[0]
        for extra in got[1:]:
            arrived = arrived + extra
        value = jnp.where(index < stride, value, arrived)
    return value


def binary_levels(size):
    levels = []
    for stride, radix in tree_levels(size):
        if radix & (radix - 1) == 0:
            while radix > 1:
                levels.append((stride, 2))
                stride *= 2
                radix //= 2
        else:
            levels.append((stride, radix))
    return levels


def spread_levels(size):
    levels = tree_levels(size)
    stride, radix = levels[-1]
    if radix > 4 and radix % 4 == 0:
        levels = levels[:-1] + [(stride, 4), (stride * 4, radix // 4)]
    return levels


def total_levels(size):
    levels = tree_levels(size)
    if len(levels) < 2:
        return levels
    inner = levels[-1][0]
    return [(1, inner), (inner, size // inner)]


def tree_total(value, axis):
    size = lax.axis_size(axis)
    for stride, radix in reversed(total_levels(size)):
        got = [
            lax.ppermute(value, axis, [(j + k * stride, j) for j in range(stride)])
            for k in range(1, radix)
        ]
        for extra in got:
            value = value + extra
    return value


def passed_along(block, axis, distance):
    devices = range(lax.axis_size(axis))
    route = [(i - distance, i) for i in devices if i - distance in devices]
    return lax.ppermute(block, axis, route)


def visible_mask(tile_id, tile_ids, listed, lengths):
    position = jnp.arange(TILE, dtype=jnp.int32)
    slot_ok = jnp.concatenate(
        [jnp.arange(PROMPT_TILES, dtype=jnp.int32) < tile_id, listed >= 0, jnp.ones((1,), bool)]
    )
    key_len = jnp.take(lengths, jnp.maximum(tile_ids, 0))
    key_ok = slot_ok[:, None] & (position[None, :] < key_len[:, None])
    own_slot = jnp.arange(KEYT) == KEYT - 1
    causal = position[None, None, :] <= position[:, None, None]
    allowed = key_ok[None, :, :] & (causal | ~own_slot[None, :, None])
    return allowed.reshape(TILE, KEYT * TILE)


def tile_backward(queries, grads_out, key_block, value_block, allowed, live_rows, scaling):
    scores = (
        jnp.einsum("igrd,jgd->grij", queries, key_block, preferred_element_type=jnp.float32)
        * scaling
    )
    scores = jnp.where(allowed, scores, -jnp.inf)
    row_max = jnp.max(scores, axis=-1, keepdims=True)
    log_total = row_max + jnp.log(jnp.sum(jnp.exp(scores - row_max), axis=-1, keepdims=True))
    weights = jnp.where(allowed & live_rows[:, None], jnp.exp(scores - log_total), 0.0)
    weight_grads = jnp.einsum(
        "igrd,jgd->grij", grads_out, value_block, preferred_element_type=jnp.float32
    )
    row_dot = jnp.sum(weights * weight_grads, axis=-1, keepdims=True)
    score_grads = (weights * (weight_grads - row_dot)).astype(jnp.bfloat16)
    weights_low = weights.astype(jnp.bfloat16)
    query_part = (
        jnp.einsum("grij,jgd->igrd", score_grads, key_block, preferred_element_type=jnp.float32)
        * scaling
    )
    key_part = jnp.einsum(
        "grij,igrd->jgd", score_grads, queries, preferred_element_type=jnp.float32
    )
    value_part = jnp.einsum(
        "grij,igrd->jgd", weights_low, grads_out, preferred_element_type=jnp.float32
    )
    return (query_part.astype(jnp.bfloat16), key_part, value_part)


def tiles_kernel(q_ref, g_ref, k_ref, v_ref, pos_ref, live_ref, dq_ref, dk_ref, dv_ref, *, group, scaling):
    keys = k_ref[0]
    values = v_ref[0]
    width = keys.shape[1]
    rows = lax.broadcasted_iota(jnp.int32, (q_ref.shape[0], keys.shape[0]), 0)
    seen = jnp.concatenate([pos_ref[0] <= rows] * group, axis=0)
    live = jnp.concatenate([live_ref[0] > 0] * group, axis=0)
    queries = jnp.concatenate([q_ref[:, r * width : (r + 1) * width] for r in range(group)], axis=0)
    grads = jnp.concatenate([g_ref[:, r * width : (r + 1) * width] for r in range(group)], axis=0)
    scores = lax.dot_general(queries, keys, (((1,), (1,)), ((), ())), preferred_element_type=jnp.float32)
    scores = jnp.where(seen, scores * scaling, -jnp.inf)
    row_max = jnp.max(scores, axis=1, keepdims=True)
    raised = jnp.exp(scores - row_max)
    inverse = 1.0 / jnp.sum(raised, axis=1, keepdims=True)
    weights = jnp.where(live, raised * inverse, 0.0)
    weight_grads = lax.dot_general(grads, values, (((1,), (1,)), ((), ())), preferred_element_type=jnp.float32)
    row_dot = jnp.sum(weights * weight_grads, axis=1, keepdims=True)
    score_grads = (weights * (weight_grads - row_dot)).astype(jnp.bfloat16)
    weights_low = weights.astype(jnp.bfloat16)
    dq = jnp.dot(score_grads, keys, preferred_element_type=jnp.float32) * scaling
    rows_q = q_ref.shape[0]
    for r in range(group):
        dq_ref[:, r * width : (r + 1) * width] = dq[r * rows_q : (r + 1) * rows_q].astype(dq_ref.dtype)
    dk_ref[0] = lax.dot_general(score_grads, queries, (((0,), (0,)), ((), ())), preferred_element_type=jnp.float32)
    dv_ref[0] = lax.dot_general(weights_low, grads, (((0,), (0,)), ((), ())), preferred_element_type=jnp.float32)


def tiles_backward(queries, grads_out, keys, values, positions, live, scaling, interpret=False):
    tiles, key_slots, width = keys.shape
    group = queries.shape[1] // width
    rows = queries.shape[0] // tiles
    row_spec = pl.BlockSpec((rows, queries.shape[1]), lambda t: (t, 0))
    key_spec = pl.BlockSpec((1, key_slots, width), lambda t: (t, 0, 0))
    kernel = lambda *refs: tiles_kernel(*refs, group=group, scaling=scaling)
    return pl.pallas_call(
        kernel,
        grid=(tiles,),
        in_specs=[
            row_spec,
            row_spec,
            key_spec,
            key_spec,
            pl.BlockSpec((1, 1, key_slots), lambda t: (t, 0, 0)),
            pl.BlockSpec((1, rows, 1), lambda t: (t, 0, 0)),
        ],
        out_specs=[row_spec, key_spec, key_spec],
        out_shape=[
            jax.ShapeDtypeStruct(queries.shape, jnp.bfloat16),
            jax.ShapeDtypeStruct(keys.shape, jnp.float32),
            jax.ShapeDtypeStruct(keys.shape, jnp.float32),
        ],
        interpret=interpret,
    )(queries, grads_out, keys, values, positions, live)


def column_limits(tile_id, tile_ids, listed, lengths):
    position = jnp.arange(TILE, dtype=jnp.int32)
    slot_ok = jnp.concatenate(
        [jnp.arange(PROMPT_TILES, dtype=jnp.int32) < tile_id, listed >= 0, jnp.ones((1,), bool)]
    )
    key_len = jnp.take(lengths, jnp.maximum(tile_ids, 0))
    key_ok = slot_ok[:, None] & (position[None, :] < key_len[:, None])
    own_slot = (jnp.arange(KEYT) == KEYT - 1)[:, None]
    limit = jnp.where(key_ok, jnp.where(own_slot, position[None, :], 0), TILE)
    return limit.reshape(1, KEYT * TILE)


def shards(query_rows, key_rows, value_rows, out_grads, lengths, ancestors):
    head_groups = lax.axis_size("head")
    width_q = query_rows.shape[1] // head_groups
    width_k = key_rows.shape[1] // head_groups
    rows_in = query_rows.shape[0]
    packed = jnp.concatenate(
        [
            query_rows.reshape(rows_in, head_groups, width_q),
            key_rows.reshape(rows_in, head_groups, width_k),
            value_rows.reshape(rows_in, head_groups, width_k),
            out_grads.reshape(rows_in, head_groups, width_q),
        ],
        axis=2,
    )
    moved = lax.all_to_all(packed, "head", split_axis=1, concat_axis=0, tiled=True)
    moved = moved.reshape(moved.shape[0], moved.shape[2])
    head_query = moved[:, :width_q]
    head_key = moved[:, width_q : width_q + width_k]
    head_value = moved[:, width_q + width_k : width_q + 2 * width_k]
    head_grad = moved[:, width_q + 2 * width_k :]
    row_count = head_query.shape[0]
    tiles_here = row_count // TILE
    kv_width = head_key.shape[1]
    kv_heads = kv_width // HD
    group_size = head_query.shape[1] // kv_width
    scaling = HD ** (-0.5)
    block_index = lax.axis_index("blk")
    first_tile = block_index * tiles_here
    window_first = (block_index - SPAN_DEV) * tiles_here
    window_slots = (SPAN_DEV + 1) * tiles_here
    own_states = jnp.concatenate(
        [
            head_key.reshape(tiles_here, TILE, kv_width),
            head_value.reshape(tiles_here, TILE, kv_width),
        ],
        axis=2,
    )
    my_lists = lax.dynamic_slice_in_dim(ancestors, first_tile, tiles_here, 0)
    prompt_ids = jnp.arange(PROMPT_TILES, dtype=jnp.int32)
    pieces = [tree_spread(own_states[:PROMPT_TILES], "blk")]
    for offset in range(SPAN_DEV, 0, -1):
        pieces.append(passed_along(own_states, "blk", offset))
    pieces.append(own_states)
    table = jnp.concatenate(pieces, axis=0)
    slot_index = jnp.arange(window_slots, dtype=jnp.int32)
    prompt_sum = jnp.zeros((PROMPT_TILES, TILE, 2 * kv_width), jnp.float32)
    near_sum = jnp.zeros((window_slots, TILE * 2 * kv_width), jnp.float32)
    key_blocks, value_blocks, limits, lives, window_rows = [], [], [], [], []
    for local in range(tiles_here):
        tile_id = first_tile + local
        listed = my_lists[local]
        tile_ids = jnp.concatenate([prompt_ids, listed, tile_id[None]])
        near_rows = jnp.where(listed >= 0, PROMPT_TILES + listed - window_first, 0)
        own_row = jnp.full((1,), PROMPT_TILES + SPAN_DEV * tiles_here + local, jnp.int32)
        table_rows = jnp.concatenate([prompt_ids, near_rows, own_row])
        chosen = jnp.take(table, table_rows, axis=0)
        key_blocks.append(chosen[:, :, :kv_width].reshape(KEYT * TILE, kv_width))
        value_blocks.append(chosen[:, :, kv_width:].reshape(KEYT * TILE, kv_width))
        limits.append(column_limits(tile_id, tile_ids, listed, lengths))
        lives.append((jnp.arange(TILE, dtype=jnp.int32) < lengths[tile_id]).astype(jnp.int32)[:, None])
        window_rows.append(listed)
    query_out, key_parts, value_parts = tiles_backward(
        head_query,
        head_grad,
        jnp.stack(key_blocks),
        jnp.stack(value_blocks),
        jnp.stack(limits),
        jnp.stack(lives),
        scaling,
    )
    for local in range(tiles_here):
        listed = window_rows[local]
        tile_terms = jnp.concatenate(
            [
                key_parts[local].reshape(KEYT, TILE, kv_width),
                value_parts[local].reshape(KEYT, TILE, kv_width),
            ],
            axis=2,
        )
        prompt_sum = prompt_sum + tile_terms[:PROMPT_TILES]
        window_ids = jnp.concatenate(
            [listed - window_first, jnp.full((1,), SPAN_DEV * tiles_here + local, jnp.int32)]
        )
        usable = jnp.concatenate([listed >= 0, jnp.ones((1,), bool)])
        placing = ((window_ids[:, None] == slot_index[None, :]) & usable[:, None]).astype(
            jnp.float32
        )
        near_sum = near_sum + jnp.einsum(
            "sw,sx->wx",
            placing,
            tile_terms[PROMPT_TILES:].reshape(ANC + 1, TILE * 2 * kv_width),
            precision=lax.Precision.HIGHEST,
        )
    root_total = tree_total(prompt_sum, "blk")
    near_parts = near_sum.reshape(SPAN_DEV + 1, tiles_here, TILE, 2 * kv_width)
    total = near_parts[SPAN_DEV]
    for offset in range(1, SPAN_DEV + 1):
        total = total + passed_along(near_parts[SPAN_DEV - offset], "blk", -offset)
    total = total.at[:PROMPT_TILES].add(jnp.where(block_index == 0, root_total, 0.0))
    key_out = (total[:, :, :kv_width] * scaling).astype(jnp.bfloat16).reshape(row_count, kv_width)
    value_out = total[:, :, kv_width:].astype(jnp.bfloat16).reshape(row_count, kv_width)
    joined = jnp.concatenate([query_out, key_out, value_out], axis=1)
    joined = joined.reshape(joined.shape[0], 1, joined.shape[1])
    back = lax.all_to_all(joined, "head", split_axis=0, concat_axis=1, tiled=True)
    rows_out = back.shape[0]
    query_grads = back[:, :, :width_q].reshape(rows_out, head_groups * width_q)
    key_grads = back[:, :, width_q : width_q + width_k].reshape(rows_out, head_groups * width_k)
    value_grads = back[:, :, width_q + width_k :].reshape(rows_out, head_groups * width_k)
    return (query_grads, key_grads, value_grads)


def solution(mesh):
    placed = (
        P(("blk", "head"), None),
        P(("blk", "head"), None),
        P(("blk", "head"), None),
        P(("blk", "head"), None),
        P(),
        P(),
    )
    return jax.shard_map(
        shards,
        mesh=mesh,
        in_specs=placed,
        out_specs=(P(("blk", "head"), None), P(("blk", "head"), None), P(("blk", "head"), None)),
        check_vma=False,
    )
```
